128 devices in a mesh: gy: 16 (over z_lo, x, core), gx: 8 (over z_hi, y).
Axes of the slice: x: 4, y: 4, z: 4 (z_hi: 2, z_lo: 2; z = z_hi * 2 + z_lo), core: 2. Of those that a mesh axis runs over, the one named last changes fastest.
Arguments:
- inputs: bfloat16 [1, 1024, 512, 384], P(None, 'gy', 'gx'), may hold values from -6 to 6
- nearby_kernel: bfloat16 [3, 3, 384, 384], replicated, may hold values from -0.109375 to 0.109375
- nearby_bias: float32 [384], replicated, may hold values from -3 to 3
- distant_kernel: bfloat16 [3, 3, 384, 384], replicated, may hold values from -0.109375 to 0.109375
- distant_bias: float32 [384], replicated, may hold values from -3 to 3
Outputs:
- outputs: bfloat16 [1, 1024, 512, 384], P(None, 'gy', 'gx')
The draws below stay inside these ranges and needn't reach their ends.
All inputs are finite; a program needn't handle non-finite values.
Results may differ from the reference program's by a relative error of at most 0.004.
Values may be sent and summed in bfloat16 or wider, within the bound.
No kernel may reach another device: no remote copies, remote signals or barrier semaphores. Data moves between devices by JAX's collectives and lax.ppermute only.
A program may use at most 128 MiB of HBM per device.

```python
import jax
import jax.numpy as jnp
from jax import lax

C = 384
NEAR_DILATION = 4
FAR_DILATION = 64
BATCH = 1
H = 1024
W = 512


def block_levels(stream_key, shape, shards, low, high):
    gain = 1.0
    for dim, shards_of in shards:
        steps = jax.random.uniform(jax.random.fold_in(jax.random.fold_in(stream_key, 6), dim), (shards_of,), jnp.float32, low / len(shards), high / len(shards))
        gain = gain * jnp.repeat(jnp.exp(steps), shape[dim] // shards_of).reshape((-1,) + (1,) * (len(shape) - 1 - dim))
    return gain


def centred(own_key, shape, deviation, bound, pieces=(), kind=jnp.bfloat16):
    factor_of = block_levels(own_key, shape, pieces, -0.22, 0.18) if pieces else 1.0
    values = jax.random.normal(own_key, shape, jnp.float32) * deviation * factor_of
    return jnp.minimum(jnp.maximum(values, -bound), bound).astype(kind)


def setup_inputs(seed: int = 0) -> dict:
    key_list = jax.random.split(jax.random.key(seed), 6)
    return {
        "inputs": centred(key_list[0], (BATCH, H, W, C), 1.0, 6.0, ((1, 16), (2, 8))),
        "nearby_kernel": centred(key_list[1], (3, 3, C, C), (9 * C) ** -0.5, 0.109375),
        "nearby_bias": centred(key_list[2], (C,), 0.5, 3.0, (), jnp.float32),
        "distant_kernel": centred(key_list[3], (3, 3, C, C), (9 * C) ** -0.5, 0.109375),
        "distant_bias": centred(key_list[4], (C,), 0.5, 3.0, (), jnp.float32),
    }


def apply_convolution(input_field, kernel_weight, dilation_rate):
    return lax.conv_general_dilated(input_field.astype(jnp.float32), kernel_weight.astype(jnp.float32), (1, 1), ((dilation_rate, dilation_rate), (dilation_rate, dilation_rate)), rhs_dilation=(dilation_rate, dilation_rate), dimension_numbers=("NHWC", "HWIO", "NHWC"), precision=lax.Precision.HIGHEST)


def reference(inputs, nearby_kernel, nearby_bias, distant_kernel, distant_bias):
    hidden_state = jax.nn.gelu(apply_convolution(inputs, nearby_kernel, NEAR_DILATION) + nearby_bias, approximate=False).astype(jnp.bfloat16)
    branch_output = jax.nn.gelu(apply_convolution(hidden_state, distant_kernel, FAR_DILATION) + distant_bias, approximate=False).astype(jnp.bfloat16)
    return (inputs.astype(jnp.float32) + branch_output.astype(jnp.float32)).astype(jnp.bfloat16)
```

```python
import jax
import jax.numpy as jnp
from jax import lax
from jax.sharding import PartitionSpec as P

NEAR_DILATION = 4
FAR_DILATION = 64
CHUNKS = 4


def shift_pairs(axis):
    size = lax.axis_size(axis)
    up = [(i, i + 1) for i in range(size - 1)]
    down = [(j, i) for i, j in up]
    return up, down


def padded(shard, sides, width):
    for axis, dim in sides:
        length = shard.shape[dim]
        up, down = shift_pairs(axis)
        last = lax.slice_in_dim(shard, length - width, length, axis=dim)
        initial = lax.slice_in_dim(shard, 0, width, axis=dim)
        before = lax.ppermute(last, axis, up)
        after = lax.ppermute(initial, axis, down)
        shard = jnp.concatenate([before, shard, after], axis=dim)
    return shard


def dilated_output(padded_input, kernel_weight, dilation_rate):
    return lax.conv_general_dilated(
        padded_input,
        kernel_weight,
        (1, 1),
        "VALID",
        rhs_dilation=(dilation_rate, dilation_rate),
        dimension_numbers=("NHWC", "HWIO", "NHWC"),
        preferred_element_type=jnp.float32,
    )


def on_device(inputs, nearby_kernel, nearby_bias, distant_kernel, distant_bias):
    batch_size, row_count, column_count, channel_count = inputs.shape
    assert row_count == FAR_DILATION and column_count == FAR_DILATION
    padded_input = padded(inputs, (("gy", 1), ("gx", 2)), NEAR_DILATION)
    halo = 2 * NEAR_DILATION
    step = row_count // CHUNKS
    x_up, x_down = shift_pairs("gx")
    y_up, y_down = shift_pairs("gy")
    far = distant_kernel.transpose(1, 2, 0, 3).reshape(3, channel_count, 3 * channel_count)
    outs = []
    for c in range(CHUNKS):
        piece = lax.slice_in_dim(padded_input, c * step, c * step + step + halo, axis=1)
        hidden = jax.nn.gelu(
            dilated_output(piece, nearby_kernel, NEAR_DILATION) + nearby_bias, approximate=False
        ).astype(jnp.bfloat16)
        hidden = hidden.reshape(batch_size * step * column_count, channel_count)
        left = lax.ppermute(hidden, "gx", x_up)
        right = lax.ppermute(hidden, "gx", x_down)
        partial = jnp.dot(hidden, far[1], preferred_element_type=jnp.float32)
        partial = partial + jnp.dot(left, far[0], preferred_element_type=jnp.float32)
        partial = partial + jnp.dot(right, far[2], preferred_element_type=jnp.float32)
        upper = lax.ppermute(partial[:, :channel_count], "gy", y_up)
        lower = lax.ppermute(partial[:, 2 * channel_count:], "gy", y_down)
        far_sum = partial[:, channel_count:2 * channel_count] + upper + lower + distant_bias
        branch = jax.nn.gelu(far_sum, approximate=False).astype(jnp.bfloat16)
        branch = branch.reshape(batch_size, step, column_count, channel_count)
        own = lax.slice_in_dim(inputs, c * step, (c + 1) * step, axis=1)
        outs.append((own.astype(jnp.float32) + branch.astype(jnp.float32)).astype(jnp.bfloat16))
    return jnp.concatenate(outs, axis=1)


def solution(mesh):
    placed = (P(None, "gy", "gx", None), P(), P(), P(), P())
    return jax.shard_map(
        on_device, mesh=mesh, in_specs=placed, out_specs=P(None, "gy", "gx", None), check_vma=False
    )
```

```python
import jax
import jax.numpy as jnp
from jax import lax
from jax.sharding import PartitionSpec as P

NEAR_DILATION = 4
FAR_DILATION = 64
CHUNK_ROWS = (15, 18, 17, 14)


def shift_pairs(axis):
    size = lax.axis_size(axis)
    up = [(i, i + 1) for i in range(size - 1)]
    down = [(j, i) for i, j in up]
    return up, down


def padded(shard, sides, width):
    for axis, dim in sides:
        length = shard.shape[dim]
        up, down = shift_pairs(axis)
        last = lax.slice_in_dim(shard, length - width, length, axis=dim)
        initial = lax.slice_in_dim(shard, 0, width, axis=dim)
        before = lax.ppermute(last, axis, up)
        after = lax.ppermute(initial, axis, down)
        shard = jnp.concatenate([before, shard, after], axis=dim)
    return shard


def dilated_output(padded_input, kernel_weight, dilation_rate):
    return lax.conv_general_dilated(
        padded_input,
        kernel_weight,
        (1, 1),
        "VALID",
        rhs_dilation=(dilation_rate, dilation_rate),
        dimension_numbers=("NHWC", "HWIO", "NHWC"),
        preferred_element_type=jnp.float32,
    )


def on_device(inputs, nearby_kernel, nearby_bias, distant_kernel, distant_bias):
    batch_size, row_count, column_count, channel_count = inputs.shape
    assert row_count == FAR_DILATION and column_count == FAR_DILATION
    padded_input = padded(inputs, (("gy", 1), ("gx", 2)), NEAR_DILATION)
    halo = 2 * NEAR_DILATION
    assert sum(CHUNK_ROWS) == row_count
    starts = [sum(CHUNK_ROWS[:c]) for c in range(len(CHUNK_ROWS))]
    x_up, x_down = shift_pairs("gx")
    y_up, y_down = shift_pairs("gy")
    far = distant_kernel.transpose(1, 2, 0, 3).reshape(3, channel_count, 3 * channel_count)
    outs = []
    hiddens = []
    for start, step in zip(starts, CHUNK_ROWS):
        piece = lax.slice_in_dim(padded_input, start, start + step + halo, axis=1)
        hidden = jax.nn.gelu(
            dilated_output(piece, nearby_kernel, NEAR_DILATION) + nearby_bias, approximate=False
        ).astype(jnp.bfloat16)
        hiddens.append(hidden.reshape(batch_size * step * column_count, channel_count))
    for hidden, start, step in zip(hiddens, starts, CHUNK_ROWS):
        left = lax.ppermute(hidden, "gx", x_up)
        right = lax.ppermute(hidden, "gx", x_down)
        partial = jnp.dot(hidden, far[1], preferred_element_type=jnp.float32)
        partial = partial + jnp.dot(left, far[0], preferred_element_type=jnp.float32)
        partial = partial + jnp.dot(right, far[2], preferred_element_type=jnp.float32)
        upper = lax.ppermute(partial[:, :channel_count].astype(jnp.bfloat16), "gy", y_up)
        lower = lax.ppermute(partial[:, 2 * channel_count:].astype(jnp.bfloat16), "gy", y_down)
        far_sum = (
            partial[:, channel_count:2 * channel_count]
            + upper.astype(jnp.float32)
            + lower.astype(jnp.float32)
            + distant_bias
        )
        branch = jax.nn.gelu(far_sum, approximate=False).astype(jnp.bfloat16)
        branch = branch.reshape(batch_size, step, column_count, channel_count)
        own = lax.slice_in_dim(inputs, start, start + step, axis=1)
        outs.append((own.astype(jnp.float32) + branch.astype(jnp.float32)).astype(jnp.bfloat16))
    return jnp.concatenate(outs, axis=1)


def solution(mesh):
    placed = (P(None, "gy", "gx", None), P(), P(), P(), P())
    return jax.shard_map(
        on_device, mesh=mesh, in_specs=placed, out_specs=P(None, "gy", "gx", None), check_vma=False
    )
```

```python
import jax
import jax.numpy as jnp
from jax import lax
from jax.sharding import PartitionSpec as P

NEAR_DILATION = 4
FAR_DILATION = 64
CHUNK_ROWS = (31, 33)


def shift_pairs(axis):
    size = lax.axis_size(axis)
    up = [(i, i + 1) for i in range(size - 1)]
    down = [(j, i) for i, j in up]
    return up, down


def padded(shard, sides, width):
    for axis, dim in sides:
        length = shard.shape[dim]
        up, down = shift_pairs(axis)
        last = lax.slice_in_dim(shard, length - width, length, axis=dim)
        initial = lax.slice_in_dim(shard, 0, width, axis=dim)
        before = lax.ppermute(last, axis, up)
        after = lax.ppermute(initial, axis, down)
        shard = jnp.concatenate([before, shard, after], axis=dim)
    return shard


def dilated_output(padded_input, kernel_weight, dilation_rate):
    return lax.conv_general_dilated(
        padded_input,
        kernel_weight,
        (1, 1),
        "VALID",
        rhs_dilation=(dilation_rate, dilation_rate),
        dimension_numbers=("NHWC", "HWIO", "NHWC"),
        preferred_element_type=jnp.float32,
    )


def on_device(inputs, nearby_kernel, nearby_bias, distant_kernel, distant_bias):
    batch_size, row_count, column_count, channel_count = inputs.shape
    assert row_count == FAR_DILATION and column_count == FAR_DILATION
    padded_input = padded(inputs, (("gy", 1), ("gx", 2)), NEAR_DILATION)
    halo = 2 * NEAR_DILATION
    assert sum(CHUNK_ROWS) == row_count
    starts = [sum(CHUNK_ROWS[:c]) for c in range(len(CHUNK_ROWS))]
    x_up, x_down = shift_pairs("gx")
    y_up, y_down = shift_pairs("gy")
    far = distant_kernel.transpose(1, 2, 0, 3).reshape(3, channel_count, 3 * channel_count)
    outs = []
    hiddens = []
    for start, step in zip(starts, CHUNK_ROWS):
        piece = lax.slice_in_dim(padded_input, start, start + step + halo, axis=1)
        hidden = jax.nn.gelu(
            dilated_output(piece, nearby_kernel, NEAR_DILATION) + nearby_bias, approximate=False
        ).astype(jnp.bfloat16)
        hiddens.append(hidden.reshape(batch_size * step * column_count, channel_count))
    for hidden, start, step in zip(hiddens, starts, CHUNK_ROWS):
        left = lax.ppermute(hidden, "gx", x_up)
        right = lax.ppermute(hidden, "gx", x_down)
        partial = jnp.dot(hidden, far[1], preferred_element_type=jnp.float32)
        partial = partial + jnp.dot(left, far[0], preferred_element_type=jnp.float32)
        partial = partial + jnp.dot(right, far[2], preferred_element_type=jnp.float32)
        upper = lax.ppermute(partial[:, :channel_count].astype(jnp.bfloat16), "gy", y_up)
        lower = lax.ppermute(partial[:, 2 * channel_count:].astype(jnp.bfloat16), "gy", y_down)
        far_sum = (
            partial[:, channel_count:2 * channel_count]
            + upper.astype(jnp.float32)
            + lower.astype(jnp.float32)
            + distant_bias
        )
        branch = jax.nn.gelu(far_sum, approximate=False).astype(jnp.bfloat16)
        branch = branch.reshape(batch_size, step, column_count, channel_count)
        own = lax.slice_in_dim(inputs, start, start + step, axis=1)
        outs.append((own.astype(jnp.float32) + branch.astype(jnp.float32)).astype(jnp.bfloat16))
    return jnp.concatenate(outs, axis=1)


def solution(mesh):
    placed = (P(None, "gy", "gx", None), P(), P(), P(), P())
    return jax.shard_map(
        on_device, mesh=mesh, in_specs=placed, out_specs=P(None, "gy", "gx", None), check_vma=False
    )
```

```python
import jax
import jax.numpy as jnp
from jax import lax
from jax.sharding import PartitionSpec as P

NEAR_DILATION = 4
FAR_DILATION = 64
CHUNK_ROWS = (15, 18, 17, 14)


def shift_pairs(axis):
    size = lax.axis_size(axis)
    up = [(i, i + 1) for i in range(size - 1)]
    down = [(j, i) for i, j in up]
    return up, down


def padded(shard, sides, width):
    for axis, dim in sides:
        length = shard.shape[dim]
        up, down = shift_pairs(axis)
        last = lax.slice_in_dim(shard, length - width, length, axis=dim)
        initial = lax.slice_in_dim(shard, 0, width, axis=dim)
        before = lax.ppermute(last, axis, up)
        after = lax.ppermute(initial, axis, down)
        shard = jnp.concatenate([before, shard, after], axis=dim)
    return shard


def dilated_output(padded_input, kernel_weight, dilation_rate):
    return lax.conv_general_dilated(
        padded_input,
        kernel_weight,
        (1, 1),
        "VALID",
        rhs_dilation=(dilation_rate, dilation_rate),
        dimension_numbers=("NHWC", "HWIO", "NHWC"),
        preferred_element_type=jnp.float32,
    )


def on_device(inputs, nearby_kernel, nearby_bias, distant_kernel, distant_bias):
    batch_size, row_count, column_count, channel_count = inputs.shape
    assert row_count == FAR_DILATION and column_count == FAR_DILATION
    width = NEAR_DILATION
    columns = padded(inputs, (("gx", 2),), width)
    y_up, y_down = shift_pairs("gy")
    above = lax.ppermute(lax.slice_in_dim(columns, row_count - width, row_count, axis=1), "gy", y_up)
    below = lax.ppermute(lax.slice_in_dim(columns, 0, width, axis=1), "gy", y_down)
    assert sum(CHUNK_ROWS) == row_count
    starts = [sum(CHUNK_ROWS[:c]) for c in range(len(CHUNK_ROWS))]
    x_up, x_down = shift_pairs("gx")
    far = distant_kernel.transpose(1, 2, 0, 3).reshape(3, channel_count, 3 * channel_count)
    outs = []
    hiddens = []
    for start, step in zip(starts, CHUNK_ROWS):
        low, high = start - width, start + step + width
        piece = lax.slice_in_dim(columns, max(low, 0), min(high, row_count), axis=1)
        if low < 0:
            piece = jnp.concatenate([above, piece], axis=1)
        if high > row_count:
            piece = jnp.concatenate([piece, below], axis=1)
        hidden = jax.nn.gelu(
            dilated_output(piece, nearby_kernel, NEAR_DILATION) + nearby_bias, approximate=False
        ).astype(jnp.bfloat16)
        hiddens.append(hidden.reshape(batch_size * step * column_count, channel_count))
    for hidden, start, step in zip(hiddens, starts, CHUNK_ROWS):
        left = lax.ppermute(hidden, "gx", x_up)
        right = lax.ppermute(hidden, "gx", x_down)
        partial = jnp.dot(hidden, far[1], preferred_element_type=jnp.float32)
        partial = partial + jnp.dot(left, far[0], preferred_element_type=jnp.float32)
        partial = partial + jnp.dot(right, far[2], preferred_element_type=jnp.float32)
        upper = lax.ppermute(partial[:, :channel_count].astype(jnp.bfloat16), "gy", y_up)
        lower = lax.ppermute(partial[:, 2 * channel_count:].astype(jnp.bfloat16), "gy", y_down)
        far_sum = (
            partial[:, channel_count:2 * channel_count]
            + upper.astype(jnp.float32)
            + lower.astype(jnp.float32)
            + distant_bias
        )
        branch = jax.nn.gelu(far_sum, approximate=False).astype(jnp.bfloat16)
        branch = branch.reshape(batch_size, step, column_count, channel_count)
        own = lax.slice_in_dim(inputs, start, start + step, axis=1)
        outs.append((own.astype(jnp.float32) + branch.astype(jnp.float32)).astype(jnp.bfloat16))
    return jnp.concatenate(outs, axis=1)


def solution(mesh):
    placed = (P(None, "gy", "gx", None), P(), P(), P(), P())
    return jax.shard_map(
        on_device, mesh=mesh, in_specs=placed, out_specs=P(None, "gy", "gx", None), check_vma=False
    )
```

```python
import jax
import jax.numpy as jnp
from jax import lax
from jax.sharding import PartitionSpec as P

NEAR_DILATION = 4
FAR_DILATION = 64
CHUNK_ROWS = (15, 18, 17, 14)


def shift_pairs(axis):
    size = lax.axis_size(axis)
    up = [(i, i + 1) for i in range(size - 1)]
    down = [(j, i) for i, j in up]
    return up, down


def padded(shard, sides, width):
    for axis, dim in sides:
        length = shard.shape[dim]
        up, down = shift_pairs(axis)
        last = lax.slice_in_dim(shard, length - width, length, axis=dim)
        initial = lax.slice_in_dim(shard, 0, width, axis=dim)
        before = lax.ppermute(last, axis, up)
        after = lax.ppermute(initial, axis, down)
        shard = jnp.concatenate([before, shard, after], axis=dim)
    return shard


def dilated_output(padded_input, kernel_weight, dilation_rate):
    return lax.conv_general_dilated(
        padded_input,
        kernel_weight,
        (1, 1),
        "VALID",
        rhs_dilation=(dilation_rate, dilation_rate),
        dimension_numbers=("NHWC", "HWIO", "NHWC"),
        preferred_element_type=jnp.float32,
    )


def on_device(inputs, nearby_kernel, nearby_bias, distant_kernel, distant_bias):
    batch_size, row_count, column_count, channel_count = inputs.shape
    assert row_count == FAR_DILATION and column_count == FAR_DILATION
    width = NEAR_DILATION
    columns = padded(inputs, (("gx", 2),), width)
    y_up, y_down = shift_pairs("gy")
    above = lax.ppermute(lax.slice_in_dim(columns, row_count - width, row_count, axis=1), "gy", y_up)
    below = lax.ppermute(lax.slice_in_dim(columns, 0, width, axis=1), "gy", y_down)
    assert sum(CHUNK_ROWS) == row_count
    starts = [sum(CHUNK_ROWS[:c]) for c in range(len(CHUNK_ROWS))]
    x_up, x_down = shift_pairs("gx")
    far = distant_kernel.transpose(1, 2, 0, 3).reshape(3, channel_count, 3 * channel_count)
    near = nearby_kernel.reshape(3, 3 * channel_count, channel_count)
    outs = []
    hiddens = []
    for start, step in zip(starts, CHUNK_ROWS):
        low, high = start - width, start + step + width
        piece = lax.slice_in_dim(columns, max(low, 0), min(high, row_count), axis=1)
        if low < 0:
            piece = jnp.concatenate([above, piece], axis=1)
        if high > row_count:
            piece = jnp.concatenate([piece, below], axis=1)
        stacked = jnp.concatenate(
            [lax.slice_in_dim(piece, e * width, e * width + column_count, axis=2) for e in range(3)],
            axis=3,
        )
        near_sum = None
        for a in range(3):
            rows = lax.slice_in_dim(stacked, a * width, a * width + step, axis=1)
            rows = rows.reshape(batch_size * step * column_count, 3 * channel_count)
            term = jnp.dot(rows, near[a], preferred_element_type=jnp.float32)
            near_sum = term if near_sum is None else near_sum + term
        hidden = jax.nn.gelu(near_sum + nearby_bias, approximate=False).astype(jnp.bfloat16)
        hiddens.append(hidden)
    for hidden, start, step in zip(hiddens, starts, CHUNK_ROWS):
        left = lax.ppermute(hidden, "gx", x_up)
        right = lax.ppermute(hidden, "gx", x_down)
        partial = jnp.dot(hidden, far[1], preferred_element_type=jnp.float32)
        partial = partial + jnp.dot(left, far[0], preferred_element_type=jnp.float32)
        partial = partial + jnp.dot(right, far[2], preferred_element_type=jnp.float32)
        upper = lax.ppermute(partial[:, :channel_count].astype(jnp.bfloat16), "gy", y_up)
        lower = lax.ppermute(partial[:, 2 * channel_count:].astype(jnp.bfloat16), "gy", y_down)
        far_sum = (
            partial[:, channel_count:2 * channel_count]
            + upper.astype(jnp.float32)
            + lower.astype(jnp.float32)
            + distant_bias
        )
        branch = jax.nn.gelu(far_sum, approximate=False).astype(jnp.bfloat16)
        branch = branch.reshape(batch_size, step, column_count, channel_count)
        own = lax.slice_in_dim(inputs, start, start + step, axis=1)
        outs.append((own.astype(jnp.float32) + branch.astype(jnp.float32)).astype(jnp.bfloat16))
    return jnp.concatenate(outs, axis=1)


def solution(mesh):
    placed = (P(None, "gy", "gx", None), P(), P(), P(), P())
    return jax.shard_map(
        on_device, mesh=mesh, in_specs=placed, out_specs=P(None, "gy", "gx", None), check_vma=False
    )
```

```python
import jax
import jax.numpy as jnp
import numpy as np
from jax import lax
from jax.sharding import PartitionSpec as P

NEAR_DILATION = 4
FAR_DILATION = 64
CHUNK_ROWS = (15, 18, 17, 14)


def shift_pairs(axis):
    size = lax.axis_size(axis)
    up = [(i, i + 1) for i in range(size - 1)]
    down = [(j, i) for i, j in up]
    return up, down


def padded(shard, sides, width):
    for axis, dim in sides:
        length = shard.shape[dim]
        up, down = shift_pairs(axis)
        last = lax.slice_in_dim(shard, length - width, length, axis=dim)
        initial = lax.slice_in_dim(shard, 0, width, axis=dim)
        before = lax.ppermute(last, axis, up)
        after = lax.ppermute(initial, axis, down)
        shard = jnp.concatenate([before, shard, after], axis=dim)
    return shard


def gelu(v):
    return 0.5 * v * (1.0 + lax.erf(v * np.float32(np.sqrt(0.5))))


def dilated_output(padded_input, kernel_weight, dilation_rate):
    return lax.conv_general_dilated(
        padded_input,
        kernel_weight,
        (1, 1),
        "VALID",
        rhs_dilation=(dilation_rate, dilation_rate),
        dimension_numbers=("NHWC", "HWIO", "NHWC"),
        preferred_element_type=jnp.float32,
    )


def on_device(inputs, nearby_kernel, nearby_bias, distant_kernel, distant_bias):
    batch_size, row_count, column_count, channel_count = inputs.shape
    assert row_count == FAR_DILATION and column_count == FAR_DILATION
    width = NEAR_DILATION
    columns = padded(inputs, (("gx", 2),), width)
    y_up, y_down = shift_pairs("gy")
    above = lax.ppermute(lax.slice_in_dim(columns, row_count - width, row_count, axis=1), "gy", y_up)
    below = lax.ppermute(lax.slice_in_dim(columns, 0, width, axis=1), "gy", y_down)
    assert sum(CHUNK_ROWS) == row_count
    starts = [sum(CHUNK_ROWS[:c]) for c in range(len(CHUNK_ROWS))]
    x_up, x_down = shift_pairs("gx")
    far = distant_kernel.transpose(1, 2, 0, 3).reshape(3, channel_count, 3 * channel_count)
    outs = []
    hiddens = []
    for start, step in zip(starts, CHUNK_ROWS):
        low, high = start - width, start + step + width
        piece = lax.slice_in_dim(columns, max(low, 0), min(high, row_count), axis=1)
        if low < 0:
            piece = jnp.concatenate([above, piece], axis=1)
        if high > row_count:
            piece = jnp.concatenate([piece, below], axis=1)
        hidden = gelu(
            dilated_output(piece, nearby_kernel, NEAR_DILATION) + nearby_bias
        ).astype(jnp.bfloat16)
        hiddens.append(hidden.reshape(batch_size * step * column_count, channel_count))
    for hidden, start, step in zip(hiddens, starts, CHUNK_ROWS):
        left = lax.ppermute(hidden, "gx", x_up)
        right = lax.ppermute(hidden, "gx", x_down)
        partial = jnp.dot(hidden, far[1], preferred_element_type=jnp.float32)
        partial = partial + jnp.dot(left, far[0], preferred_element_type=jnp.float32)
        partial = partial + jnp.dot(right, far[2], preferred_element_type=jnp.float32)
        upper = lax.ppermute(partial[:, :channel_count].astype(jnp.bfloat16), "gy", y_up)
        lower = lax.ppermute(partial[:, 2 * channel_count:].astype(jnp.bfloat16), "gy", y_down)
        far_sum = (
            partial[:, channel_count:2 * channel_count]
            + upper.astype(jnp.float32)
            + lower.astype(jnp.float32)
            + distant_bias
        )
        branch = gelu(far_sum).astype(jnp.bfloat16)
        branch = branch.reshape(batch_size, step, column_count, channel_count)
        own = lax.slice_in_dim(inputs, start, start + step, axis=1)
        outs.append((own.astype(jnp.float32) + branch.astype(jnp.float32)).astype(jnp.bfloat16))
    return jnp.concatenate(outs, axis=1)


def solution(mesh):
    placed = (P(None, "gy", "gx", None), P(), P(), P(), P())
    return jax.shard_map(
        on_device, mesh=mesh, in_specs=placed, out_specs=P(None, "gy", "gx", None), check_vma=False
    )
```

```python
import jax
import jax.numpy as jnp
import numpy as np
from jax import lax
from jax.sharding import PartitionSpec as P

NEAR_DILATION = 4
FAR_DILATION = 64
CHUNK_ROWS = (20, 23, 21)


def shift_pairs(axis):
    size = lax.axis_size(axis)
    up = [(i, i + 1) for i in range(size - 1)]
    down = [(j, i) for i, j in up]
    return up, down


def padded(shard, sides, width):
    for axis, dim in sides:
        length = shard.shape[dim]
        up, down = shift_pairs(axis)
        last = lax.slice_in_dim(shard, length - width, length, axis=dim)
        initial = lax.slice_in_dim(shard, 0, width, axis=dim)
        before = lax.ppermute(last, axis, up)
        after = lax.ppermute(initial, axis, down)
        shard = jnp.concatenate([before, shard, after], axis=dim)
    return shard


def gelu(v):
    return 0.5 * v * (1.0 + lax.erf(v * np.float32(np.sqrt(0.5))))


def dilated_output(padded_input, kernel_weight, dilation_rate):
    return lax.conv_general_dilated(
        padded_input,
        kernel_weight,
        (1, 1),
        "VALID",
        rhs_dilation=(dilation_rate, dilation_rate),
        dimension_numbers=("NHWC", "HWIO", "NHWC"),
        preferred_element_type=jnp.float32,
    )


def on_device(inputs, nearby_kernel, nearby_bias, distant_kernel, distant_bias):
    batch_size, row_count, column_count, channel_count = inputs.shape
    assert row_count == FAR_DILATION and column_count == FAR_DILATION
    width = NEAR_DILATION
    columns = padded(inputs, (("gx", 2),), width)
    y_up, y_down = shift_pairs("gy")
    above = lax.ppermute(lax.slice_in_dim(columns, row_count - width, row_count, axis=1), "gy", y_up)
    below = lax.ppermute(lax.slice_in_dim(columns, 0, width, axis=1), "gy", y_down)
    assert sum(CHUNK_ROWS) == row_count
    starts = [sum(CHUNK_ROWS[:c]) for c in range(len(CHUNK_ROWS))]
    x_up, x_down = shift_pairs("gx")
    far = distant_kernel.transpose(1, 2, 0, 3).reshape(3, channel_count, 3 * channel_count)
    outs = []
    hiddens = []
    for start, step in zip(starts, CHUNK_ROWS):
        low, high = start - width, start + step + width
        piece = lax.slice_in_dim(columns, max(low, 0), min(high, row_count), axis=1)
        if low < 0:
            piece = jnp.concatenate([above, piece], axis=1)
        if high > row_count:
            piece = jnp.concatenate([piece, below], axis=1)
        hidden = gelu(
            dilated_output(piece, nearby_kernel, NEAR_DILATION) + nearby_bias
        ).astype(jnp.bfloat16)
        hiddens.append(hidden.reshape(batch_size * step * column_count, channel_count))
    for hidden, start, step in zip(hiddens, starts, CHUNK_ROWS):
        left = lax.ppermute(hidden, "gx", x_up)
        right = lax.ppermute(hidden, "gx", x_down)
        partial = jnp.dot(hidden, far[1], preferred_element_type=jnp.float32)
        partial = partial + jnp.dot(left, far[0], preferred_element_type=jnp.float32)
        partial = partial + jnp.dot(right, far[2], preferred_element_type=jnp.float32)
        upper = lax.ppermute(partial[:, :channel_count].astype(jnp.bfloat16), "gy", y_up)
        lower = lax.ppermute(partial[:, 2 * channel_count:].astype(jnp.bfloat16), "gy", y_down)
        far_sum = (
            partial[:, channel_count:2 * channel_count]
            + upper.astype(jnp.float32)
            + lower.astype(jnp.float32)
            + distant_bias
        )
        branch = gelu(far_sum).astype(jnp.bfloat16)
        branch = branch.reshape(batch_size, step, column_count, channel_count)
        own = lax.slice_in_dim(inputs, start, start + step, axis=1)
        outs.append((own.astype(jnp.float32) + branch.astype(jnp.float32)).astype(jnp.bfloat16))
    return jnp.concatenate(outs, axis=1)


def solution(mesh):
    placed = (P(None, "gy", "gx", None), P(), P(), P(), P())
    return jax.shard_map(
        on_device, mesh=mesh, in_specs=placed, out_specs=P(None, "gy", "gx", None), check_vma=False
    )
```

```python
import jax
import jax.numpy as jnp
import numpy as np
from jax import lax
from jax.sharding import PartitionSpec as P

NEAR_DILATION = 4
FAR_DILATION = 64
CHUNK_ROWS = (22, 27, 15)


def shift_pairs(axis):
    size = lax.axis_size(axis)
    up = [(i, i + 1) for i in range(size - 1)]
    down = [(j, i) for i, j in up]
    return up, down


def padded(shard, sides, width):
    for axis, dim in sides:
        length = shard.shape[dim]
        up, down = shift_pairs(axis)
        last = lax.slice_in_dim(shard, length - width, length, axis=dim)
        initial = lax.slice_in_dim(shard, 0, width, axis=dim)
        before = lax.ppermute(last, axis, up)
        after = lax.ppermute(initial, axis, down)
        shard = jnp.concatenate([before, shard, after], axis=dim)
    return shard


def gelu(v):
    return 0.5 * v * (1.0 + lax.erf(v * np.float32(np.sqrt(0.5))))


def dilated_output(padded_input, kernel_weight, dilation_rate):
    return lax.conv_general_dilated(
        padded_input,
        kernel_weight,
        (1, 1),
        "VALID",
        rhs_dilation=(dilation_rate, dilation_rate),
        dimension_numbers=("NHWC", "HWIO", "NHWC"),
        preferred_element_type=jnp.float32,
    )


def on_device(inputs, nearby_kernel, nearby_bias, distant_kernel, distant_bias):
    batch_size, row_count, column_count, channel_count = inputs.shape
    assert row_count == FAR_DILATION and column_count == FAR_DILATION
    width = NEAR_DILATION
    columns = padded(inputs, (("gx", 2),), width)
    y_up, y_down = shift_pairs("gy")
    above = lax.ppermute(lax.slice_in_dim(columns, row_count - width, row_count, axis=1), "gy", y_up)
    below = lax.ppermute(lax.slice_in_dim(columns, 0, width, axis=1), "gy", y_down)
    assert sum(CHUNK_ROWS) == row_count
    starts = [sum(CHUNK_ROWS[:c]) for c in range(len(CHUNK_ROWS))]
    x_up, x_down = shift_pairs("gx")
    far = distant_kernel.transpose(1, 2, 0, 3).reshape(3, channel_count, 3 * channel_count)
    outs = []
    hiddens = []
    for start, step in zip(starts, CHUNK_ROWS):
        low, high = start - width, start + step + width
        piece = lax.slice_in_dim(columns, max(low, 0), min(high, row_count), axis=1)
        if low < 0:
            piece = jnp.concatenate([above, piece], axis=1)
        if high > row_count:
            piece = jnp.concatenate([piece, below], axis=1)
        hidden = gelu(
            dilated_output(piece, nearby_kernel, NEAR_DILATION) + nearby_bias
        ).astype(jnp.bfloat16)
        hiddens.append(hidden.reshape(batch_size * step * column_count, channel_count))
    for hidden, start, step in zip(hiddens, starts, CHUNK_ROWS):
        left = lax.ppermute(hidden, "gx", x_up)
        right = lax.ppermute(hidden, "gx", x_down)
        partial = jnp.dot(hidden, far[1], preferred_element_type=jnp.float32)
        partial = partial + jnp.dot(left, far[0], preferred_element_type=jnp.float32)
        partial = partial + jnp.dot(right, far[2], preferred_element_type=jnp.float32)
        upper = lax.ppermute(partial[:, :channel_count].astype(jnp.bfloat16), "gy", y_up)
        lower = lax.ppermute(partial[:, 2 * channel_count:].astype(jnp.bfloat16), "gy", y_down)
        far_sum = (
            partial[:, channel_count:2 * channel_count]
            + upper.astype(jnp.float32)
            + lower.astype(jnp.float32)
            + distant_bias
        )
        branch = gelu(far_sum).astype(jnp.bfloat16)
        branch = branch.reshape(batch_size, step, column_count, channel_count)
        own = lax.slice_in_dim(inputs, start, start + step, axis=1)
        outs.append((own.astype(jnp.float32) + branch.astype(jnp.float32)).astype(jnp.bfloat16))
    return jnp.concatenate(outs, axis=1)


def solution(mesh):
    placed = (P(None, "gy", "gx", None), P(), P(), P(), P())
    return jax.shard_map(
        on_device, mesh=mesh, in_specs=placed, out_specs=P(None, "gy", "gx", None), check_vma=False
    )
```

```python
import jax
import jax.numpy as jnp
import numpy as np
from jax import lax
from jax.sharding import PartitionSpec as P

NEAR_DILATION = 4
FAR_DILATION = 64
CHUNK_ROWS = (30, 34)


def shift_pairs(axis):
    size = lax.axis_size(axis)
    up = [(i, i + 1) for i in range(size - 1)]
    down = [(j, i) for i, j in up]
    return up, down


def padded(shard, sides, width):
    for axis, dim in sides:
        length = shard.shape[dim]
        up, down = shift_pairs(axis)
        last = lax.slice_in_dim(shard, length - width, length, axis=dim)
        initial = lax.slice_in_dim(shard, 0, width, axis=dim)
        before = lax.ppermute(last, axis, up)
        after = lax.ppermute(initial, axis, down)
        shard = jnp.concatenate([before, shard, after], axis=dim)
    return shard


def gelu(v):
    return 0.5 * v * (1.0 + lax.erf(v * np.float32(np.sqrt(0.5))))


def dilated_output(padded_input, kernel_weight, dilation_rate):
    return lax.conv_general_dilated(
        padded_input,
        kernel_weight,
        (1, 1),
        "VALID",
        rhs_dilation=(dilation_rate, dilation_rate),
        dimension_numbers=("NHWC", "HWIO", "NHWC"),
        preferred_element_type=jnp.float32,
    )


def on_device(inputs, nearby_kernel, nearby_bias, distant_kernel, distant_bias):
    batch_size, row_count, column_count, channel_count = inputs.shape
    assert row_count == FAR_DILATION and column_count == FAR_DILATION
    width = NEAR_DILATION
    columns = padded(inputs, (("gx", 2),), width)
    y_up, y_down = shift_pairs("gy")
    above = lax.ppermute(lax.slice_in_dim(columns, row_count - width, row_count, axis=1), "gy", y_up)
    below = lax.ppermute(lax.slice_in_dim(columns, 0, width, axis=1), "gy", y_down)
    assert sum(CHUNK_ROWS) == row_count
    starts = [sum(CHUNK_ROWS[:c]) for c in range(len(CHUNK_ROWS))]
    x_up, x_down = shift_pairs("gx")
    far = distant_kernel.transpose(1, 2, 0, 3).reshape(3, channel_count, 3 * channel_count)
    outs = []
    hiddens = []
    for start, step in zip(starts, CHUNK_ROWS):
        low, high = start - width, start + step + width
        piece = lax.slice_in_dim(columns, max(low, 0), min(high, row_count), axis=1)
        if low < 0:
            piece = jnp.concatenate([above, piece], axis=1)
        if high > row_count:
            piece = jnp.concatenate([piece, below], axis=1)
        hidden = gelu(
            dilated_output(piece, nearby_kernel, NEAR_DILATION) + nearby_bias
        ).astype(jnp.bfloat16)
        hiddens.append(hidden.reshape(batch_size * step * column_count, channel_count))
    for hidden, start, step in zip(hiddens, starts, CHUNK_ROWS):
        left = lax.ppermute(hidden, "gx", x_up)
        right = lax.ppermute(hidden, "gx", x_down)
        partial = jnp.dot(hidden, far[1], preferred_element_type=jnp.float32)
        partial = partial + jnp.dot(left, far[0], preferred_element_type=jnp.float32)
        partial = partial + jnp.dot(right, far[2], preferred_element_type=jnp.float32)
        upper = lax.ppermute(partial[:, :channel_count].astype(jnp.bfloat16), "gy", y_up)
        lower = lax.ppermute(partial[:, 2 * channel_count:].astype(jnp.bfloat16), "gy", y_down)
        far_sum = (
            partial[:, channel_count:2 * channel_count]
            + upper.astype(jnp.float32)
            + lower.astype(jnp.float32)
            + distant_bias
        )
        branch = gelu(far_sum).astype(jnp.bfloat16)
        branch = branch.reshape(batch_size, step, column_count, channel_count)
        own = lax.slice_in_dim(inputs, start, start + step, axis=1)
        outs.append((own.astype(jnp.float32) + branch.astype(jnp.float32)).astype(jnp.bfloat16))
    return jnp.concatenate(outs, axis=1)


def solution(mesh):
    placed = (P(None, "gy", "gx", None), P(), P(), P(), P())
    return jax.shard_map(
        on_device, mesh=mesh, in_specs=placed, out_specs=P(None, "gy", "gx", None), check_vma=False
    )
```

```python
import jax
import jax.numpy as jnp
import numpy as np
from jax import lax
from jax.sharding import PartitionSpec as P

NEAR_DILATION = 4
FAR_DILATION = 64
CHUNK_ROWS = (20, 23, 21)


def shift_pairs(axis):
    size = lax.axis_size(axis)
    up = [(i, i + 1) for i in range(size - 1)]
    down = [(j, i) for i, j in up]
    return up, down


def pair_swaps(axis):
    size = lax.axis_size(axis)
    first = [(i, i ^ 1) for i in range(size) if i ^ 1 < size]
    second = [(i, i + 1) for i in range(1, size - 1, 2)]
    second += [(j, i) for i, j in second]
    return first, second


def padded(shard, sides, width):
    for axis, dim in sides:
        length = shard.shape[dim]
        up, down = shift_pairs(axis)
        last = lax.slice_in_dim(shard, length - width, length, axis=dim)
        initial = lax.slice_in_dim(shard, 0, width, axis=dim)
        before = lax.ppermute(last, axis, up)
        after = lax.ppermute(initial, axis, down)
        shard = jnp.concatenate([before, shard, after], axis=dim)
    return shard


def gelu(v):
    return 0.5 * v * (1.0 + lax.erf(v * np.float32(np.sqrt(0.5))))


def dilated_output(padded_input, kernel_weight, dilation_rate):
    return lax.conv_general_dilated(
        padded_input,
        kernel_weight,
        (1, 1),
        "VALID",
        rhs_dilation=(dilation_rate, dilation_rate),
        dimension_numbers=("NHWC", "HWIO", "NHWC"),
        preferred_element_type=jnp.float32,
    )


def on_device(inputs, nearby_kernel, nearby_bias, distant_kernel, distant_bias):
    batch_size, row_count, column_count, channel_count = inputs.shape
    assert row_count == FAR_DILATION and column_count == FAR_DILATION
    width = NEAR_DILATION
    columns = padded(inputs, (("gx", 2),), width)
    y_up, y_down = shift_pairs("gy")
    above = lax.ppermute(lax.slice_in_dim(columns, row_count - width, row_count, axis=1), "gy", y_up)
    below = lax.ppermute(lax.slice_in_dim(columns, 0, width, axis=1), "gy", y_down)
    assert sum(CHUNK_ROWS) == row_count
    starts = [sum(CHUNK_ROWS[:c]) for c in range(len(CHUNK_ROWS))]
    x_first, x_second = pair_swaps("gx")
    y_first, y_second = pair_swaps("gy")
    x_even = lax.axis_index("gx") % 2 == 0
    y_even = lax.axis_index("gy") % 2 == 0
    far = distant_kernel.transpose(1, 2, 0, 3).reshape(3, channel_count, 3 * channel_count)
    weights = (far[1], jnp.where(x_even, far[2], far[0]), jnp.where(x_even, far[0], far[2]))
    def by_row_parity(w):
        flipped = jnp.concatenate(
            [w[:, 2 * channel_count:], w[:, channel_count:2 * channel_count], w[:, :channel_count]], axis=1
        )
        return jnp.where(y_even, w, flipped)
    weights = [by_row_parity(w) for w in weights]
    outs = []
    hiddens = []
    for start, step in zip(starts, CHUNK_ROWS):
        low, high = start - width, start + step + width
        piece = lax.slice_in_dim(columns, max(low, 0), min(high, row_count), axis=1)
        if low < 0:
            piece = jnp.concatenate([above, piece], axis=1)
        if high > row_count:
            piece = jnp.concatenate([piece, below], axis=1)
        hidden = gelu(
            dilated_output(piece, nearby_kernel, NEAR_DILATION) + nearby_bias
        ).astype(jnp.bfloat16)
        hiddens.append(hidden.reshape(batch_size * step * column_count, channel_count))
    for hidden, start, step in zip(hiddens, starts, CHUNK_ROWS):
        near_side = lax.ppermute(hidden, "gx", x_first)
        far_side = lax.ppermute(hidden, "gx", x_second)
        partial = jnp.dot(hidden, weights[0], preferred_element_type=jnp.float32)
        partial = partial + jnp.dot(near_side, weights[1], preferred_element_type=jnp.float32)
        partial = partial + jnp.dot(far_side, weights[2], preferred_element_type=jnp.float32)
        upper = lax.ppermute(partial[:, :channel_count].astype(jnp.bfloat16), "gy", y_first)
        lower = lax.ppermute(partial[:, 2 * channel_count:].astype(jnp.bfloat16), "gy", y_second)
        far_sum = (
            partial[:, channel_count:2 * channel_count]
            + upper.astype(jnp.float32)
            + lower.astype(jnp.float32)
            + distant_bias
        )
        branch = gelu(far_sum).astype(jnp.bfloat16)
        branch = branch.reshape(batch_size, step, column_count, channel_count)
        own = lax.slice_in_dim(inputs, start, start + step, axis=1)
        outs.append((own.astype(jnp.float32) + branch.astype(jnp.float32)).astype(jnp.bfloat16))
    return jnp.concatenate(outs, axis=1)


def solution(mesh):
    placed = (P(None, "gy", "gx", None), P(), P(), P(), P())
    return jax.shard_map(
        on_device, mesh=mesh, in_specs=placed, out_specs=P(None, "gy", "gx", None), check_vma=False
    )
```

```python
import jax
import jax.numpy as jnp
import numpy as np
from jax import lax
from jax.sharding import PartitionSpec as P

NEAR_DILATION = 4
FAR_DILATION = 64
CHUNK_ROWS = (15, 18, 17, 14)


def shift_pairs(axis):
    size = lax.axis_size(axis)
    up = [(i, i + 1) for i in range(size - 1)]
    down = [(j, i) for i, j in up]
    return up, down


def pair_swaps(axis):
    size = lax.axis_size(axis)
    first = [(i, i ^ 1) for i in range(size) if i ^ 1 < size]
    second = [(i, i + 1) for i in range(1, size - 1, 2)]
    second += [(j, i) for i, j in second]
    return first, second


def padded(shard, sides, width):
    for axis, dim in sides:
        length = shard.shape[dim]
        up, down = shift_pairs(axis)
        last = lax.slice_in_dim(shard, length - width, length, axis=dim)
        initial = lax.slice_in_dim(shard, 0, width, axis=dim)
        before = lax.ppermute(last, axis, up)
        after = lax.ppermute(initial, axis, down)
        shard = jnp.concatenate([before, shard, after], axis=dim)
    return shard


def gelu(v):
    return 0.5 * v * (1.0 + lax.erf(v * np.float32(np.sqrt(0.5))))


def dilated_output(padded_input, kernel_weight, dilation_rate):
    return lax.conv_general_dilated(
        padded_input,
        kernel_weight,
        (1, 1),
        "VALID",
        rhs_dilation=(dilation_rate, dilation_rate),
        dimension_numbers=("NHWC", "HWIO", "NHWC"),
        preferred_element_type=jnp.float32,
    )


def on_device(inputs, nearby_kernel, nearby_bias, distant_kernel, distant_bias):
    batch_size, row_count, column_count, channel_count = inputs.shape
    assert row_count == FAR_DILATION and column_count == FAR_DILATION
    width = NEAR_DILATION
    columns = padded(inputs, (("gx", 2),), width)
    y_up, y_down = shift_pairs("gy")
    above = lax.ppermute(lax.slice_in_dim(columns, row_count - width, row_count, axis=1), "gy", y_up)
    below = lax.ppermute(lax.slice_in_dim(columns, 0, width, axis=1), "gy", y_down)
    assert sum(CHUNK_ROWS) == row_count
    starts = [sum(CHUNK_ROWS[:c]) for c in range(len(CHUNK_ROWS))]
    x_first, x_second = pair_swaps("gx")
    y_first, y_second = pair_swaps("gy")
    x_even = lax.axis_index("gx") % 2 == 0
    y_even = lax.axis_index("gy") % 2 == 0
    far = distant_kernel.transpose(1, 2, 0, 3).reshape(3, channel_count, 3 * channel_count)
    weights = (far[1], jnp.where(x_even, far[2], far[0]), jnp.where(x_even, far[0], far[2]))
    def by_row_parity(w):
        flipped = jnp.concatenate(
            [w[:, 2 * channel_count:], w[:, channel_count:2 * channel_count], w[:, :channel_count]], axis=1
        )
        return jnp.where(y_even, w, flipped)
    weights = [by_row_parity(w) for w in weights]
    outs = []
    hiddens = []
    for start, step in zip(starts, CHUNK_ROWS):
        low, high = start - width, start + step + width
        piece = lax.slice_in_dim(columns, max(low, 0), min(high, row_count), axis=1)
        if low < 0:
            piece = jnp.concatenate([above, piece], axis=1)
        if high > row_count:
            piece = jnp.concatenate([piece, below], axis=1)
        hidden = gelu(
            dilated_output(piece, nearby_kernel, NEAR_DILATION) + nearby_bias
        ).astype(jnp.bfloat16)
        hiddens.append(hidden.reshape(batch_size * step * column_count, channel_count))
    for hidden, start, step in zip(hiddens, starts, CHUNK_ROWS):
        near_side = lax.ppermute(hidden, "gx", x_first)
        far_side = lax.ppermute(hidden, "gx", x_second)
        partial = jnp.dot(hidden, weights[0], preferred_element_type=jnp.float32)
        partial = partial + jnp.dot(near_side, weights[1], preferred_element_type=jnp.float32)
        partial = partial + jnp.dot(far_side, weights[2], preferred_element_type=jnp.float32)
        upper = lax.ppermute(partial[:, :channel_count].astype(jnp.bfloat16), "gy", y_first)
        lower = lax.ppermute(partial[:, 2 * channel_count:].astype(jnp.bfloat16), "gy", y_second)
        far_sum = (
            partial[:, channel_count:2 * channel_count]
            + upper.astype(jnp.float32)
            + lower.astype(jnp.float32)
            + distant_bias
        )
        branch = gelu(far_sum).astype(jnp.bfloat16)
        branch = branch.reshape(batch_size, step, column_count, channel_count)
        own = lax.slice_in_dim(inputs, start, start + step, axis=1)
        outs.append((own.astype(jnp.float32) + branch.astype(jnp.float32)).astype(jnp.bfloat16))
    return jnp.concatenate(outs, axis=1)


def solution(mesh):
    placed = (P(None, "gy", "gx", None), P(), P(), P(), P())
    return jax.shard_map(
        on_device, mesh=mesh, in_specs=placed, out_specs=P(None, "gy", "gx", None), check_vma=False
    )
```

```python
import jax
import jax.numpy as jnp
import numpy as np
from jax import lax
from jax.sharding import PartitionSpec as P

NEAR_DILATION = 4
FAR_DILATION = 64
CHUNK_ROWS = (20, 23, 21)


def shift_pairs(axis):
    size = lax.axis_size(axis)
    up = [(i, i + 1) for i in range(size - 1)]
    down = [(j, i) for i, j in up]
    return up, down


def padded(shard, sides, width):
    for axis, dim in sides:
        length = shard.shape[dim]
        up, down = shift_pairs(axis)
        last = lax.slice_in_dim(shard, length - width, length, axis=dim)
        initial = lax.slice_in_dim(shard, 0, width, axis=dim)
        before = lax.ppermute(last, axis, up)
        after = lax.ppermute(initial, axis, down)
        shard = jnp.concatenate([before, shard, after], axis=dim)
    return shard


def gelu(v):
    return 0.5 * v * (1.0 + lax.erf(v * np.float32(np.sqrt(0.5))))


def dilated_output(padded_input, kernel_weight, dilation_rate):
    return lax.conv_general_dilated(
        padded_input,
        kernel_weight,
        (1, 1),
        "VALID",
        rhs_dilation=(dilation_rate, dilation_rate),
        dimension_numbers=("NHWC", "HWIO", "NHWC"),
        preferred_element_type=jnp.float32,
    )


def on_device(inputs, nearby_kernel, nearby_bias, distant_kernel, distant_bias):
    batch_size, row_count, column_count, channel_count = inputs.shape
    assert row_count == FAR_DILATION and column_count == FAR_DILATION
    width = NEAR_DILATION
    columns = padded(inputs, (("gx", 2),), width)
    y_up, y_down = shift_pairs("gy")
    above = lax.ppermute(lax.slice_in_dim(columns, row_count - width, row_count, axis=1), "gy", y_up)
    below = lax.ppermute(lax.slice_in_dim(columns, 0, width, axis=1), "gy", y_down)
    assert sum(CHUNK_ROWS) == row_count
    starts = [sum(CHUNK_ROWS[:c]) for c in range(len(CHUNK_ROWS))]
    x_up, x_down = shift_pairs("gx")
    far = distant_kernel.transpose(1, 2, 0, 3).reshape(3, channel_count, 3 * channel_count)
    result = jnp.zeros_like(inputs)
    hiddens = []
    for start, step in zip(starts, CHUNK_ROWS):
        low, high = start - width, start + step + width
        piece = lax.slice_in_dim(columns, max(low, 0), min(high, row_count), axis=1)
        if low < 0:
            piece = jnp.concatenate([above, piece], axis=1)
        if high > row_count:
            piece = jnp.concatenate([piece, below], axis=1)
        hidden = gelu(
            dilated_output(piece, nearby_kernel, NEAR_DILATION) + nearby_bias
        ).astype(jnp.bfloat16)
        hiddens.append(hidden.reshape(batch_size * step * column_count, channel_count))
    for hidden, start, step in zip(hiddens, starts, CHUNK_ROWS):
        left = lax.ppermute(hidden, "gx", x_up)
        right = lax.ppermute(hidden, "gx", x_down)
        partial = jnp.dot(hidden, far[1], preferred_element_type=jnp.float32)
        partial = partial + jnp.dot(left, far[0], preferred_element_type=jnp.float32)
        partial = partial + jnp.dot(right, far[2], preferred_element_type=jnp.float32)
        upper = lax.ppermute(partial[:, :channel_count].astype(jnp.bfloat16), "gy", y_up)
        lower = lax.ppermute(partial[:, 2 * channel_count:].astype(jnp.bfloat16), "gy", y_down)
        far_sum = (
            partial[:, channel_count:2 * channel_count]
            + upper.astype(jnp.float32)
            + lower.astype(jnp.float32)
            + distant_bias
        )
        branch = gelu(far_sum).astype(jnp.bfloat16)
        branch = branch.reshape(batch_size, step, column_count, channel_count)
        own = lax.slice_in_dim(inputs, start, start + step, axis=1)
        piece_out = (own.astype(jnp.float32) + branch.astype(jnp.float32)).astype(jnp.bfloat16)
        result = lax.dynamic_update_slice_in_dim(result, piece_out, start, axis=1)
    return result


def solution(mesh):
    placed = (P(None, "gy", "gx", None), P(), P(), P(), P())
    return jax.shard_map(
        on_device, mesh=mesh, in_specs=placed, out_specs=P(None, "gy", "gx", None), check_vma=False
    )
```

```python
import jax
import jax.numpy as jnp
import numpy as np
from jax import lax
from jax.sharding import PartitionSpec as P

NEAR_DILATION = 4
FAR_DILATION = 64
CHUNK_ROWS = (20, 23, 21)


def shift_pairs(axis):
    size = lax.axis_size(axis)
    up = [(i, i + 1) for i in range(size - 1)]
    down = [(j, i) for i, j in up]
    return up, down


def pair_swaps(axis):
    size = lax.axis_size(axis)
    first = [(i, i ^ 1) for i in range(size) if i ^ 1 < size]
    second = [(i, i + 1) for i in range(1, size - 1, 2)]
    second += [(j, i) for i, j in second]
    return first, second


def padded(shard, sides, width):
    for axis, dim in sides:
        length = shard.shape[dim]
        up, down = shift_pairs(axis)
        last = lax.slice_in_dim(shard, length - width, length, axis=dim)
        initial = lax.slice_in_dim(shard, 0, width, axis=dim)
        before = lax.ppermute(last, axis, up)
        after = lax.ppermute(initial, axis, down)
        shard = jnp.concatenate([before, shard, after], axis=dim)
    return shard


def gelu(v):
    return 0.5 * v * (1.0 + lax.erf(v * np.float32(np.sqrt(0.5))))


def dilated_output(padded_input, kernel_weight, dilation_rate):
    return lax.conv_general_dilated(
        padded_input,
        kernel_weight,
        (1, 1),
        "VALID",
        rhs_dilation=(dilation_rate, dilation_rate),
        dimension_numbers=("NHWC", "HWIO", "NHWC"),
        preferred_element_type=jnp.float32,
    )


def on_device(inputs, nearby_kernel, nearby_bias, distant_kernel, distant_bias):
    batch_size, row_count, column_count, channel_count = inputs.shape
    assert row_count == FAR_DILATION and column_count == FAR_DILATION
    width = NEAR_DILATION
    columns = padded(inputs, (("gx", 2),), width)
    y_up, y_down = shift_pairs("gy")
    above = lax.ppermute(lax.slice_in_dim(columns, row_count - width, row_count, axis=1), "gy", y_up)
    below = lax.ppermute(lax.slice_in_dim(columns, 0, width, axis=1), "gy", y_down)
    assert sum(CHUNK_ROWS) == row_count
    starts = [sum(CHUNK_ROWS[:c]) for c in range(len(CHUNK_ROWS))]
    x_up, x_down = shift_pairs("gx")
    far = distant_kernel.transpose(1, 2, 0, 3).reshape(3, channel_count, 3 * channel_count)
    y_first, y_second = pair_swaps("gy")
    y_even = lax.axis_index("gy") % 2 == 0
    flipped = jnp.concatenate(
        [far[:, :, 2 * channel_count:], far[:, :, channel_count:2 * channel_count], far[:, :, :channel_count]],
        axis=2,
    )
    far = jnp.where(y_even, far, flipped)
    outs = []
    hiddens = []
    for start, step in zip(starts, CHUNK_ROWS):
        low, high = start - width, start + step + width
        piece = lax.slice_in_dim(columns, max(low, 0), min(high, row_count), axis=1)
        if low < 0:
            piece = jnp.concatenate([above, piece], axis=1)
        if high > row_count:
            piece = jnp.concatenate([piece, below], axis=1)
        hidden = gelu(
            dilated_output(piece, nearby_kernel, NEAR_DILATION) + nearby_bias
        ).astype(jnp.bfloat16)
        hiddens.append(hidden.reshape(batch_size * step * column_count, channel_count))
    for hidden, start, step in zip(hiddens, starts, CHUNK_ROWS):
        left = lax.ppermute(hidden, "gx", x_up)
        right = lax.ppermute(hidden, "gx", x_down)
        partial = jnp.dot(hidden, far[1], preferred_element_type=jnp.float32)
        partial = partial + jnp.dot(left, far[0], preferred_element_type=jnp.float32)
        partial = partial + jnp.dot(right, far[2], preferred_element_type=jnp.float32)
        upper = lax.ppermute(partial[:, :channel_count].astype(jnp.bfloat16), "gy", y_first)
        lower = lax.ppermute(partial[:, 2 * channel_count:].astype(jnp.bfloat16), "gy", y_second)
        far_sum = (
            partial[:, channel_count:2 * channel_count]
            + upper.astype(jnp.float32)
            + lower.astype(jnp.float32)
            + distant_bias
        )
        branch = gelu(far_sum).astype(jnp.bfloat16)
        branch = branch.reshape(batch_size, step, column_count, channel_count)
        own = lax.slice_in_dim(inputs, start, start + step, axis=1)
        outs.append((own.astype(jnp.float32) + branch.astype(jnp.float32)).astype(jnp.bfloat16))
    return jnp.concatenate(outs, axis=1)


def solution(mesh):
    placed = (P(None, "gy", "gx", None), P(), P(), P(), P())
    return jax.shard_map(
        on_device, mesh=mesh, in_specs=placed, out_specs=P(None, "gy", "gx", None), check_vma=False
    )
```

```python
import jax
import jax.numpy as jnp
import numpy as np
from jax import lax
from jax.sharding import PartitionSpec as P

NEAR_DILATION = 4
FAR_DILATION = 64
INTERIOR_ROWS = 26


def shift_pairs(axis):
    size = lax.axis_size(axis)
    up = [(i, i + 1) for i in range(size - 1)]
    down = [(j, i) for i, j in up]
    return up, down


def padded(shard, sides, width):
    for axis, dim in sides:
        length = shard.shape[dim]
        up, down = shift_pairs(axis)
        last = lax.slice_in_dim(shard, length - width, length, axis=dim)
        initial = lax.slice_in_dim(shard, 0, width, axis=dim)
        before = lax.ppermute(last, axis, up)
        after = lax.ppermute(initial, axis, down)
        shard = jnp.concatenate([before, shard, after], axis=dim)
    return shard


def gelu(v):
    return 0.5 * v * (1.0 + lax.erf(v * np.float32(np.sqrt(0.5))))


def dilated_output(padded_input, kernel_weight, dilation_rate):
    return lax.conv_general_dilated(
        padded_input,
        kernel_weight,
        (1, 1),
        "VALID",
        rhs_dilation=(dilation_rate, dilation_rate),
        dimension_numbers=("NHWC", "HWIO", "NHWC"),
        preferred_element_type=jnp.float32,
    )


def on_device(inputs, nearby_kernel, nearby_bias, distant_kernel, distant_bias):
    batch_size, row_count, column_count, channel_count = inputs.shape
    assert row_count == FAR_DILATION and column_count == FAR_DILATION
    width = NEAR_DILATION
    halo = 2 * width
    x_up, x_down = shift_pairs("gx")
    y_up, y_down = shift_pairs("gy")

    def hidden_of(piece):
        near = dilated_output(piece, nearby_kernel, NEAR_DILATION) + nearby_bias
        return gelu(near).astype(jnp.bfloat16)

    def flat(v):
        return v.reshape(-1, channel_count)

    split = width + INTERIOR_ROWS
    inner = [(width, split), (split, row_count - width)]
    hiddens, owns = [], []
    for low, high in inner:
        hiddens.append(flat(hidden_of(lax.slice_in_dim(inputs, low - width, high + width, axis=1))))
        owns.append(flat(inputs[:, low:high, width:column_count - width]))
    full = padded(inputs, (("gy", 1), ("gx", 2)), width)
    strips = [
        full[:, 0:halo + width],
        full[:, row_count - width:row_count + halo],
        full[:, width:row_count + width, 0:halo + width],
        full[:, width:row_count + width, column_count - width:column_count + halo],
    ]
    hiddens.append(jnp.concatenate([flat(hidden_of(p)) for p in strips], axis=0))
    owns.append(jnp.concatenate([
        flat(inputs[:, 0:width]),
        flat(inputs[:, row_count - width:]),
        flat(inputs[:, width:row_count - width, 0:width]),
        flat(inputs[:, width:row_count - width, column_count - width:]),
    ], axis=0))
    far = distant_kernel.transpose(1, 2, 0, 3).reshape(3, channel_count, 3 * channel_count)
    outs = []
    for hidden, own in zip(hiddens, owns):
        left = lax.ppermute(hidden, "gx", x_up)
        right = lax.ppermute(hidden, "gx", x_down)
        partial = jnp.dot(hidden, far[1], preferred_element_type=jnp.float32)
        partial = partial + jnp.dot(left, far[0], preferred_element_type=jnp.float32)
        partial = partial + jnp.dot(right, far[2], preferred_element_type=jnp.float32)
        upper = lax.ppermute(partial[:, :channel_count].astype(jnp.bfloat16), "gy", y_up)
        lower = lax.ppermute(partial[:, 2 * channel_count:].astype(jnp.bfloat16), "gy", y_down)
        far_sum = (
            partial[:, channel_count:2 * channel_count]
            + upper.astype(jnp.float32)
            + lower.astype(jnp.float32)
            + distant_bias
        )
        branch = gelu(far_sum).astype(jnp.bfloat16)
        outs.append((own.astype(jnp.float32) + branch.astype(jnp.float32)).astype(jnp.bfloat16))
    inner_rows = row_count - halo
    inner_cols = column_count - halo
    interior = jnp.concatenate(
        [o.reshape(batch_size, -1, inner_cols, channel_count) for o in outs[:2]], axis=1
    )
    ring = outs[2]
    band = width * column_count
    side = inner_rows * width
    top = ring[:band].reshape(batch_size, width, column_count, channel_count)
    bottom = ring[band:2 * band].reshape(batch_size, width, column_count, channel_count)
    left = ring[2 * band:2 * band + side].reshape(batch_size, inner_rows, width, channel_count)
    right = ring[2 * band + side:].reshape(batch_size, inner_rows, width, channel_count)
    middle = jnp.concatenate([left, interior, right], axis=2)
    return jnp.concatenate([top, middle, bottom], axis=1)


def solution(mesh):
    placed = (P(None, "gy", "gx", None), P(), P(), P(), P())
    return jax.shard_map(
        on_device, mesh=mesh, in_specs=placed, out_specs=P(None, "gy", "gx", None), check_vma=False
    )
```

```python
import jax
import jax.numpy as jnp
import numpy as np
from jax import lax
from jax.sharding import PartitionSpec as P

NEAR_DILATION = 4
FAR_DILATION = 64
CHUNK_ROWS = (20, 23, 21)


def shift_pairs(axis):
    size = lax.axis_size(axis)
    up = [(i, i + 1) for i in range(size - 1)]
    down = [(j, i) for i, j in up]
    return up, down


def padded(shard, sides, width):
    for axis, dim in sides:
        length = shard.shape[dim]
        up, down = shift_pairs(axis)
        last = lax.slice_in_dim(shard, length - width, length, axis=dim)
        initial = lax.slice_in_dim(shard, 0, width, axis=dim)
        before = lax.ppermute(last, axis, up)
        after = lax.ppermute(initial, axis, down)
        shard = jnp.concatenate([before, shard, after], axis=dim)
    return shard


def gelu(v):
    return 0.5 * v * (1.0 + lax.erf(v * np.float32(np.sqrt(0.5))))


def dilated_output(padded_input, kernel_weight, dilation_rate):
    return lax.conv_general_dilated(
        padded_input,
        kernel_weight,
        (1, 1),
        "VALID",
        rhs_dilation=(dilation_rate, dilation_rate),
        dimension_numbers=("NHWC", "HWIO", "NHWC"),
        preferred_element_type=jnp.float32,
    )


def on_device(inputs, nearby_kernel, nearby_bias, distant_kernel, distant_bias):
    batch_size, row_count, column_count, channel_count = inputs.shape
    assert row_count == FAR_DILATION and column_count == FAR_DILATION
    width = NEAR_DILATION
    columns = padded(inputs, (("gx", 2),), width)
    y_up, y_down = shift_pairs("gy")
    above = lax.ppermute(lax.slice_in_dim(columns, row_count - width, row_count, axis=1), "gy", y_up)
    below = lax.ppermute(lax.slice_in_dim(columns, 0, width, axis=1), "gy", y_down)
    assert sum(CHUNK_ROWS) == row_count
    starts = [sum(CHUNK_ROWS[:c]) for c in range(len(CHUNK_ROWS))]
    x_up, x_down = shift_pairs("gx")
    outs = []
    hiddens = []
    for start, step in zip(starts, CHUNK_ROWS):
        low, high = start - width, start + step + width
        piece = lax.slice_in_dim(columns, max(low, 0), min(high, row_count), axis=1)
        if low < 0:
            piece = jnp.concatenate([above, piece], axis=1)
        if high > row_count:
            piece = jnp.concatenate([piece, below], axis=1)
        hidden = gelu(
            dilated_output(piece, nearby_kernel, NEAR_DILATION) + nearby_bias
        ).astype(jnp.bfloat16)
        hiddens.append(hidden.reshape(batch_size * step * column_count, channel_count))
    late_kernel, _ = lax.optimization_barrier((distant_kernel, hiddens[1]))
    far = late_kernel.transpose(1, 2, 0, 3).reshape(3, channel_count, 3 * channel_count)
    for hidden, start, step in zip(hiddens, starts, CHUNK_ROWS):
        left = lax.ppermute(hidden, "gx", x_up)
        right = lax.ppermute(hidden, "gx", x_down)
        partial = jnp.dot(hidden, far[1], preferred_element_type=jnp.float32)
        partial = partial + jnp.dot(left, far[0], preferred_element_type=jnp.float32)
        partial = partial + jnp.dot(right, far[2], preferred_element_type=jnp.float32)
        upper = lax.ppermute(partial[:, :channel_count].astype(jnp.bfloat16), "gy", y_up)
        lower = lax.ppermute(partial[:, 2 * channel_count:].astype(jnp.bfloat16), "gy", y_down)
        far_sum = (
            partial[:, channel_count:2 * channel_count]
            + upper.astype(jnp.float32)
            + lower.astype(jnp.float32)
            + distant_bias
        )
        branch = gelu(far_sum).astype(jnp.bfloat16)
        branch = branch.reshape(batch_size, step, column_count, channel_count)
        own = lax.slice_in_dim(inputs, start, start + step, axis=1)
        outs.append((own.astype(jnp.float32) + branch.astype(jnp.float32)).astype(jnp.bfloat16))
    return jnp.concatenate(outs, axis=1)


def solution(mesh):
    placed = (P(None, "gy", "gx", None), P(), P(), P(), P())
    return jax.shard_map(
        on_device, mesh=mesh, in_specs=placed, out_specs=P(None, "gy", "gx", None), check_vma=False
    )
```

```python
import jax
import jax.numpy as jnp
import numpy as np
from jax import lax
from jax.sharding import PartitionSpec as P

NEAR_DILATION = 4
FAR_DILATION = 64
CHUNK_ROWS = (20, 23, 21)


def shift_pairs(axis):
    size = lax.axis_size(axis)
    up = [(i, i + 1) for i in range(size - 1)]
    down = [(j, i) for i, j in up]
    return up, down


def padded(shard, sides, width):
    for axis, dim in sides:
        length = shard.shape[dim]
        up, down = shift_pairs(axis)
        last = lax.slice_in_dim(shard, length - width, length, axis=dim)
        initial = lax.slice_in_dim(shard, 0, width, axis=dim)
        before = lax.ppermute(last, axis, up)
        after = lax.ppermute(initial, axis, down)
        shard = jnp.concatenate([before, shard, after], axis=dim)
    return shard


def gelu(v):
    return 0.5 * v * (1.0 + lax.erf(v * np.float32(np.sqrt(0.5))))


def dilated_output(padded_input, kernel_weight, dilation_rate):
    return lax.conv_general_dilated(
        padded_input,
        kernel_weight,
        (1, 1),
        "VALID",
        rhs_dilation=(dilation_rate, dilation_rate),
        dimension_numbers=("NHWC", "HWIO", "NHWC"),
        preferred_element_type=jnp.float32,
    )


def on_device(inputs, nearby_kernel, nearby_bias, distant_kernel, distant_bias):
    batch_size, row_count, column_count, channel_count = inputs.shape
    assert row_count == FAR_DILATION and column_count == FAR_DILATION
    width = NEAR_DILATION
    columns = padded(inputs, (("gx", 2),), width)
    y_up, y_down = shift_pairs("gy")
    above = lax.ppermute(lax.slice_in_dim(columns, row_count - width, row_count, axis=1), "gy", y_up)
    below = lax.ppermute(lax.slice_in_dim(columns, 0, width, axis=1), "gy", y_down)
    assert sum(CHUNK_ROWS) == row_count
    starts = [sum(CHUNK_ROWS[:c]) for c in range(len(CHUNK_ROWS))]
    x_up, x_down = shift_pairs("gx")
    far = distant_kernel.transpose(1, 2, 0, 3).reshape(3, channel_count, 3 * channel_count)
    far_sent = jnp.concatenate([far[:, :, :channel_count], far[:, :, 2 * channel_count:]], axis=2)
    far_kept = far[:, :, channel_count:2 * channel_count]
    outs = []
    hiddens = []
    for start, step in zip(starts, CHUNK_ROWS):
        low, high = start - width, start + step + width
        piece = lax.slice_in_dim(columns, max(low, 0), min(high, row_count), axis=1)
        if low < 0:
            piece = jnp.concatenate([above, piece], axis=1)
        if high > row_count:
            piece = jnp.concatenate([piece, below], axis=1)
        hidden = gelu(
            dilated_output(piece, nearby_kernel, NEAR_DILATION) + nearby_bias
        ).astype(jnp.bfloat16)
        hiddens.append(hidden.reshape(batch_size * step * column_count, channel_count))
    for hidden, start, step in zip(hiddens, starts, CHUNK_ROWS):
        left = lax.ppermute(hidden, "gx", x_up)
        right = lax.ppermute(hidden, "gx", x_down)
        sent = jnp.dot(hidden, far_sent[1], preferred_element_type=jnp.float32)
        sent = sent + jnp.dot(left, far_sent[0], preferred_element_type=jnp.float32)
        sent = sent + jnp.dot(right, far_sent[2], preferred_element_type=jnp.float32)
        upper = lax.ppermute(sent[:, :channel_count].astype(jnp.bfloat16), "gy", y_up)
        lower = lax.ppermute(sent[:, channel_count:].astype(jnp.bfloat16), "gy", y_down)
        kept = jnp.dot(hidden, far_kept[1], preferred_element_type=jnp.float32)
        kept = kept + jnp.dot(left, far_kept[0], preferred_element_type=jnp.float32)
        kept = kept + jnp.dot(right, far_kept[2], preferred_element_type=jnp.float32)
        far_sum = (
            kept
            + upper.astype(jnp.float32)
            + lower.astype(jnp.float32)
            + distant_bias
        )
        branch = gelu(far_sum).astype(jnp.bfloat16)
        branch = branch.reshape(batch_size, step, column_count, channel_count)
        own = lax.slice_in_dim(inputs, start, start + step, axis=1)
        outs.append((own.astype(jnp.float32) + branch.astype(jnp.float32)).astype(jnp.bfloat16))
    return jnp.concatenate(outs, axis=1)


def solution(mesh):
    placed = (P(None, "gy", "gx", None), P(), P(), P(), P())
    return jax.shard_map(
        on_device, mesh=mesh, in_specs=placed, out_specs=P(None, "gy", "gx", None), check_vma=False
    )
```
